1024 devices in a mesh: ctx: 128 (over x, z, y_lo), dp: 8 (over y_hi, core).
Axes of the slice: x: 4, y: 8 (y_hi: 4, y_lo: 2; y = y_hi * 2 + y_lo), z: 16, core: 2. Of those that a mesh axis runs over, the one named last changes fastest.
Arguments:
- queries: bfloat16 [8, 16384, 2048], P('dp', 'ctx'), may hold values from -400 to 400
- keys: bfloat16 [8, 16384, 1024], P('dp', 'ctx'), may hold values from -400 to 400
- values: bfloat16 [8, 16384, 1024], P('dp', 'ctx'), may hold values from -6 to 6
- q_gain: float32 [256], replicated, may hold values from 0.25 to 1.75
- key_norm_gain: float32 [256], replicated, may hold values from 0.25 to 1.75
- segment_ids: int32 [8, 16384], P('dp', 'ctx'), may hold values from 0 to 63, never falling along the last dimension, each value on 1 to 1024 neighbouring positions
- output_gradient: bfloat16 [8, 16384, 2048], P('dp', 'ctx'), may hold values from -14 to 14
Outputs:
- attn_out: bfloat16 [8, 16384, 2048], P('dp', 'ctx')
- grad_queries: bfloat16 [8, 16384, 2048], P('dp', 'ctx')
- key_gradient: bfloat16 [8, 16384, 1024], P('dp', 'ctx')
- value_gradient: bfloat16 [8, 16384, 1024], P('dp', 'ctx')
- grad_q_gain: float32 [256], replicated
- grad_k_gain: float32 [256], replicated
The draws below stay inside these ranges and needn't reach their ends.
Inputs may be any that keep to these rules, and one draw needn't show every extreme that they name: `segment_ids`: document ids never fall along a sequence; every id from 0 to 63 is used, each document holds 1 to 1024 tokens and at least one holds exactly 1024.
All inputs are finite; a program needn't handle non-finite values.
Results may differ from the reference program's by a relative error of at most 0.013.
Values may be sent and summed in bfloat16 or wider, within the bound.
No kernel may reach another device: no remote copies, remote signals or barrier semaphores. Data moves between devices by JAX's collectives and lax.ppermute only.
A program may use at most 32 MiB of HBM per device.

```python
import math
from functools import partial
import jax
import jax.numpy as jnp
import numpy as np
from jax import lax

QUERY_HEADS = 8
KEY_VALUE_HEADS = 4
HEAD_SIZE = 256
WINDOW = 256
DEVICE_TOKENS = 128
HALO = 2
SEQUENCE_LENGTH = 16384
SEQUENCE_COUNT = 8
DOCS = 64
DOC_MOST = 1024
N_CTX = 128


def scaled_gradient_field(key, width):
    noise_key, col_key, row_key = jax.random.split(key, 3)
    shape = (SEQUENCE_COUNT, SEQUENCE_LENGTH, width)
    col_scale = jnp.exp(jax.random.uniform(col_key, (width,), jnp.float32, 0.0, math.log(10.0)))
    row_scale = jnp.exp(jax.random.uniform(row_key, (SEQUENCE_COUNT, SEQUENCE_LENGTH, 1), jnp.float32, 0.0, math.log(10.0)))
    base = jnp.clip(jax.random.normal(noise_key, shape, jnp.float32), -4.0, 4.0)
    return base * row_scale * col_scale


def draw_queries(key, part):
    return scaled_gradient_field(jax.random.fold_in(key, 11), QUERY_HEADS * HEAD_SIZE).astype(jnp.bfloat16)


def draw_keys(key, part):
    return scaled_gradient_field(jax.random.fold_in(key, 23), KEY_VALUE_HEADS * HEAD_SIZE).astype(jnp.bfloat16)


def draw_output_gradient(key, part):
    noise_key = jax.random.fold_in(jax.random.fold_in(key, 37), 0)
    shape = (SEQUENCE_COUNT, SEQUENCE_LENGTH, QUERY_HEADS * HEAD_SIZE)
    where_along = jnp.arange(SEQUENCE_LENGTH, dtype=jnp.float32).reshape(1, SEQUENCE_LENGTH, 1) / (SEQUENCE_LENGTH - 1)
    base = jnp.clip(jax.random.normal(noise_key, shape, jnp.float32), -4.0, 4.0)
    ramp = 1.0 + 2.0 * where_along
    return (base * ramp).astype(jnp.bfloat16)


def level_of(rng, extent, cuts, smallest, high):
    level = 1.0
    for dim, blocks in cuts:
        heights = jax.random.uniform(jax.random.fold_in(jax.random.fold_in(rng, 6), dim), (blocks,), jnp.float32, smallest / len(cuts), high / len(cuts))
        level = level * jnp.repeat(jnp.exp(heights), extent[dim] // blocks).reshape((-1,) + (1,) * (len(extent) - 1 - dim))
    return level


def profile(number_of, total, reach, lean):
    loads = [(1 << 20) // math.isqrt(grade ** lean) + 1 for grade in range(2, number_of + 1)]
    rest, counts = total - reach - (number_of - 1), [1] * (number_of - 1)
    while rest > 0:
        candidates = [i for i in range(number_of - 1) if counts[i] < reach]
        whole, left = sum([loads[i] for i in candidates]), rest
        for i in candidates:
            more = min(reach - counts[i], max(1, left * loads[i] // whole), rest)
            counts[i] = counts[i] + more
            rest = rest - more
    return np.array([reach] + counts)


def uneven(rng, count, total, limit, slope):
    if count == 2:
        one = jax.random.randint(rng, (), max(1, total - limit), min(limit, total - 1) + 1)
        return jnp.stack([one, total - one])
    lengths = jnp.asarray(profile(count, total, limit, slope), jnp.int32)
    pairs = (count - 1) // 2
    giver, taker = lengths[1:1 + 2 * pairs:2], lengths[2:2 + 2 * pairs:2]
    slack = jnp.minimum(giver - 1, limit - taker)
    passed = jax.random.randint(jax.random.fold_in(rng, 1), (pairs,), 0, 1 << 20) % (slack + 1)
    lengths = lengths.at[1:1 + 2 * pairs:2].set(giver - passed).at[2:2 + 2 * pairs:2].set(taker + passed)
    return lengths[jax.random.permutation(jax.random.fold_in(rng, 2), count)]


def scatter_about(own_key, extent, deviation, bound, cuts=(), held_as=jnp.bfloat16):
    gain = level_of(own_key, extent, cuts, -0.22, 0.18) if cuts else 1.0
    array = jax.random.normal(own_key, extent, jnp.float32) * deviation * gain
    return jnp.minimum(jnp.maximum(array, -bound), bound).astype(held_as)


def setup_inputs(seed: int = 0) -> dict:
    arg_keys = jax.random.split(jax.random.key(seed), 8)
    queries = draw_queries(jax.random.fold_in(arg_keys[7], 71), 0)
    keys = draw_keys(jax.random.fold_in(arg_keys[7], 71), 0)
    values = scatter_about(arg_keys[2], (SEQUENCE_COUNT, SEQUENCE_LENGTH, KEY_VALUE_HEADS * HEAD_SIZE), 1.0, 6.0, ((0, 8), (1, 128)))
    q_gain = jnp.clip(1.0 + 0.15 * jax.random.normal(arg_keys[3], (HEAD_SIZE,), jnp.float32), 0.25, 1.75)
    key_norm_gain = jnp.clip(1.0 + 0.15 * jax.random.normal(arg_keys[4], (HEAD_SIZE,), jnp.float32), 0.25, 1.75)
    segment_ids = jax.vmap(lambda own: jnp.searchsorted(jnp.cumsum(uneven(own, DOCS, SEQUENCE_LENGTH, DOC_MOST, 2)), jnp.arange(SEQUENCE_LENGTH), side="right"))(jax.random.split(arg_keys[5], SEQUENCE_COUNT)).reshape((SEQUENCE_COUNT, SEQUENCE_LENGTH)).astype(jnp.int32)
    output_gradient = draw_output_gradient(jax.random.fold_in(arg_keys[7], 71), 0)
    return dict(queries=queries, keys=keys, values=values, q_gain=q_gain, key_norm_gain=key_norm_gain, segment_ids=segment_ids, output_gradient=output_gradient)


EPS = 1e-06

def rms_normalize(inputs, heads, gain_vec):
    as_float = inputs.astype(jnp.float32).reshape(inputs.shape[0], heads, HEAD_SIZE)
    inv_rms = lax.rsqrt(lax.optimization_barrier(jnp.mean(as_float * as_float, -1, keepdims=True)) + EPS)
    normed = as_float * inv_rms
    return (normed, inv_rms, (normed * gain_vec).astype(jnp.bfloat16))

def rms_norm_backward(upstream, normed, inv_rms, gain_vec):
    scaled = upstream * gain_vec
    return inv_rms * (scaled - normed * lax.optimization_barrier(jnp.mean(scaled * normed, -1, keepdims=True)))

def round_down(inputs):
    return lax.optimization_barrier(inputs.astype(jnp.bfloat16))

def one_sequence(q_gain, key_norm_gain, inputs):
    queries, keys, values, segments, output_gradient = inputs
    query_group_width = QUERY_HEADS // KEY_VALUE_HEADS
    score_scale = HEAD_SIZE ** (-0.5)
    window_extent = HALO * DEVICE_TOKENS
    width_all = (HALO + 1) * DEVICE_TOKENS
    q_normed, q_inv, query_norm_result = rms_normalize(queries, QUERY_HEADS, q_gain)
    normalized_keys, key_inverse_rms, key_norm_result = rms_normalize(keys, KEY_VALUE_HEADS, key_norm_gain)
    padded_keys = jnp.concatenate([jnp.zeros((window_extent, KEY_VALUE_HEADS, HEAD_SIZE), jnp.bfloat16), key_norm_result])
    padded_values = jnp.concatenate([jnp.zeros((window_extent, KEY_VALUE_HEADS, HEAD_SIZE), jnp.bfloat16), values.reshape(SEQUENCE_LENGTH, KEY_VALUE_HEADS, HEAD_SIZE)])
    seg_padded = jnp.concatenate([jnp.full((window_extent,), -1, jnp.int32), segments.astype(jnp.int32)])
    offsets = jnp.arange(DEVICE_TOKENS, dtype=jnp.int32)
    key_offsets = jnp.arange(width_all, dtype=jnp.int32)
    distance = offsets[:, None] + window_extent - key_offsets[None, :]
    in_window = (distance >= 0) & (distance < WINDOW)
    gradient_bundle = output_gradient.reshape(SEQUENCE_LENGTH, KEY_VALUE_HEADS, query_group_width, HEAD_SIZE)

    def step(carry, shard):
        key_acc, value_accumulator, gain_acc = carry
        start = (shard * DEVICE_TOKENS).astype(jnp.int32)
        query_block = lax.dynamic_slice_in_dim(query_norm_result, start, DEVICE_TOKENS, 0)
        query_block = query_block.reshape(DEVICE_TOKENS, KEY_VALUE_HEADS, query_group_width, HEAD_SIZE).astype(jnp.float32)
        q_seg = lax.dynamic_slice_in_dim(segments.astype(jnp.int32), start, DEVICE_TOKENS, 0)
        key_block = lax.dynamic_slice_in_dim(padded_keys, start, width_all, 0).astype(jnp.float32)
        value_block = lax.dynamic_slice_in_dim(padded_values, start, width_all, 0).astype(jnp.float32)
        key_seg = lax.dynamic_slice_in_dim(seg_padded, start, width_all, 0)
        key_mask = in_window & (q_seg[:, None] == key_seg[None, :])
        scores = jnp.einsum('qhgd,khd->hgqk', query_block, key_block) * score_scale
        exp_scores = jnp.where(key_mask, jnp.exp(scores), 0.0)
        probs = exp_scores / lax.optimization_barrier(jnp.sum(exp_scores, -1, keepdims=True))
        probs_f = round_down(probs).astype(jnp.float32)
        attn_block = round_down(jnp.einsum('hgqk,khd->qhgd', probs_f, value_block))
        grad_block = lax.dynamic_slice_in_dim(gradient_bundle, start, DEVICE_TOKENS, 0).astype(jnp.float32)
        row_delta = lax.optimization_barrier(jnp.sum(grad_block * attn_block.astype(jnp.float32), -1)).transpose(1, 2, 0)
        prob_grad = jnp.einsum('qhgd,khd->hgqk', grad_block, value_block)
        score_grad = round_down(probs * (prob_grad - row_delta[..., None])).astype(jnp.float32)
        q_grad = jnp.einsum('hgqk,khd->qhgd', score_grad, key_block) * score_scale
        q_grad = q_grad.reshape(DEVICE_TOKENS, QUERY_HEADS, HEAD_SIZE)
        key_term = round_down(jnp.einsum('hgqk,qhgd->khd', score_grad, query_block) * score_scale).astype(jnp.float32)
        value_term = round_down(jnp.einsum('hgqk,qhgd->khd', probs_f, grad_block)).astype(jnp.float32)
        key_now = lax.dynamic_slice_in_dim(key_acc, start, width_all, 0)
        key_acc = lax.dynamic_update_slice_in_dim(key_acc, key_now + key_term, start, 0)
        value_now = lax.dynamic_slice_in_dim(value_accumulator, start, width_all, 0)
        value_accumulator = lax.dynamic_update_slice_in_dim(value_accumulator, value_now + value_term, start, 0)
        normed_block = lax.dynamic_slice_in_dim(q_normed, start, DEVICE_TOKENS, 0)
        inv_block = lax.dynamic_slice_in_dim(q_inv, start, DEVICE_TOKENS, 0)
        dq_block = rms_norm_backward(q_grad, normed_block, inv_block, q_gain).astype(jnp.bfloat16)
        gain_acc = gain_acc + lax.optimization_barrier(jnp.sum(q_grad * normed_block, (0, 1)))
        outputs = (attn_block.reshape(DEVICE_TOKENS, QUERY_HEADS * HEAD_SIZE), dq_block.reshape(DEVICE_TOKENS, QUERY_HEADS * HEAD_SIZE))
        return ((key_acc, value_accumulator, gain_acc), outputs)
    starting_carry = (jnp.zeros((window_extent + SEQUENCE_LENGTH, KEY_VALUE_HEADS, HEAD_SIZE), jnp.float32), jnp.zeros((window_extent + SEQUENCE_LENGTH, KEY_VALUE_HEADS, HEAD_SIZE), jnp.float32), jnp.zeros((HEAD_SIZE,), jnp.float32))
    finals, stacked = lax.scan(step, starting_carry, jnp.arange(N_CTX, dtype=jnp.int32))
    key_acc, value_accumulator, q_sum = finals
    attn_blocks, dq_blocks = stacked
    key_norm_gradient = key_acc[window_extent:]
    key_gradient = rms_norm_backward(key_norm_gradient, normalized_keys, key_inverse_rms, key_norm_gain).astype(jnp.bfloat16).reshape(SEQUENCE_LENGTH, KEY_VALUE_HEADS * HEAD_SIZE)
    value_gradient = value_accumulator[window_extent:].astype(jnp.bfloat16).reshape(SEQUENCE_LENGTH, KEY_VALUE_HEADS * HEAD_SIZE)
    k_sum = lax.optimization_barrier(jnp.sum(key_norm_gradient * normalized_keys, (0, 1)))
    return (attn_blocks.reshape(SEQUENCE_LENGTH, QUERY_HEADS * HEAD_SIZE), dq_blocks.reshape(SEQUENCE_LENGTH, QUERY_HEADS * HEAD_SIZE), key_gradient, value_gradient, q_sum, k_sum)

def reference(queries, keys, values, q_gain, key_norm_gain, segment_ids, output_gradient):
    results = lax.map(partial(one_sequence, q_gain, key_norm_gain), (queries, keys, values, segment_ids, output_gradient))
    attn_out, grad_queries, key_gradient, value_gradient, q_sums, k_sums = results
    factor = (SEQUENCE_LENGTH * SEQUENCE_COUNT) ** (-0.5)
    return (attn_out, grad_queries, key_gradient, value_gradient, lax.optimization_barrier(jnp.sum(q_sums, 0)) * factor, lax.optimization_barrier(jnp.sum(k_sums, 0)) * factor)
```

```python
import itertools
import math

import jax
import jax.numpy as jnp
from jax import lax
from jax.sharding import PartitionSpec as P

QUERY_HEADS = 8
KEY_VALUE_HEADS = 4
HEAD_SIZE = 256
WINDOW = 256
HALO = 2


EPS = 1e-06


RING_ORDER = {2: (0, 1), 4: (0, 1, 3, 2), 16: (11, 7, 12, 8, 15, 3, 0, 4, 9, 5, 10, 6, 13, 1, 14, 2)}
AXIS_PARTS = {"ctx": (4, 16, 2), "dp": (4, 2)}


def virtual_order(axis, count):
    parts = AXIS_PARTS.get(axis)
    if parts is None or count != math.prod(parts) or any(p not in RING_ORDER for p in parts):
        return list(range(count))
    order = []
    for digits in itertools.product(*[range(p) for p in parts]):
        index = 0
        for digit, size in zip(digits, parts):
            index = index * size + RING_ORDER[size][digit]
        order.append(index)
    return order


def butterfly_sum(value):
    for axis in ("dp", "ctx"):
        count = lax.axis_size(axis)
        if count & (count - 1):
            value = lax.psum(value, axis)
            continue
        device_of = virtual_order(axis, count)
        virtual_of = {device: virtual for virtual, device in enumerate(device_of)}
        bit = 1
        while bit < count:
            pairs = [(device, device_of[virtual_of[device] ^ bit]) for device in range(count)]
            value = value + lax.ppermute(value, axis, pairs)
            bit *= 2
    return value


def shifted(value, axis, by):
    count = lax.axis_size(axis)
    pairs = [(i, i + by) for i in range(count) if 0 <= i + by < count]
    return lax.ppermute(value, axis, pairs)


def rms_normalize(inputs, heads, gain_vec):
    as_float = inputs.astype(jnp.float32).reshape(inputs.shape[0], heads, HEAD_SIZE)
    inv_rms = lax.rsqrt(jnp.mean(as_float * as_float, -1, keepdims=True) + EPS)
    normed = as_float * inv_rms
    return (normed, inv_rms, (normed * gain_vec).astype(jnp.bfloat16))


def rms_norm_backward(upstream, normed, inv_rms, gain_vec):
    scaled = upstream * gain_vec
    return inv_rms * (scaled - normed * jnp.mean(scaled * normed, -1, keepdims=True))


def body(queries, keys, values, q_gain, key_norm_gain, segment_ids, output_gradient):
    token_rows = queries.shape[1]
    query_group_width = QUERY_HEADS // KEY_VALUE_HEADS
    score_scale = HEAD_SIZE ** (-0.5)
    ctx_index = lax.axis_index("ctx")
    q_normed, q_inv, query_norm_result = rms_normalize(queries[0], QUERY_HEADS, q_gain)
    normalized_keys, key_inverse_rms, key_norm_result = rms_normalize(
        keys[0], KEY_VALUE_HEADS, key_norm_gain
    )
    own_seg = segment_ids[0]
    local_key_value = jnp.stack(
        [key_norm_result.reshape(token_rows, KEY_VALUE_HEADS * HEAD_SIZE), values[0]]
    )
    received = []
    for offset in range(1, HALO + 1):
        received.append(shifted((local_key_value, own_seg), "ctx", offset))
    blocks = [received[HALO - 1 - block] for block in range(HALO)] + [(local_key_value, own_seg)]
    positions = jnp.arange(token_rows, dtype=jnp.int32)
    q_pos = ctx_index * token_rows + positions
    grouped_queries = query_norm_result.reshape(
        token_rows, KEY_VALUE_HEADS, query_group_width, HEAD_SIZE
    )
    key_block_list, value_block_list, key_masks, live_flags = ([], [], [], [])
    for block in range(HALO + 1):
        key_value_pair, seg_block = blocks[block]
        k_pos = (ctx_index - HALO + block) * token_rows + positions
        distance = q_pos[:, None] - k_pos[None, :]
        key_mask = (
            (distance >= 0)
            & (distance < WINDOW)
            & (k_pos[None, :] >= 0)
            & (own_seg[:, None] == seg_block[None, :])
        )
        key_block_list.append(key_value_pair[0].reshape(token_rows, KEY_VALUE_HEADS, HEAD_SIZE))
        value_block_list.append(key_value_pair[1].reshape(token_rows, KEY_VALUE_HEADS, HEAD_SIZE))
        key_masks.append(key_mask)
        live_flags.append(jnp.any(key_mask))
    output_shape = (token_rows, KEY_VALUE_HEADS, query_group_width, HEAD_SIZE)

    def exp_block(block):
        scores = (
            jnp.einsum(
                "qhgd,khd->hgqk",
                grouped_queries,
                key_block_list[block],
                preferred_element_type=jnp.float32,
            )
            * score_scale
        )
        return jnp.where(key_masks[block], jnp.exp(scores), 0.0)

    exp_blocks = [exp_block(block) for block in range(HALO + 1)]
    row_totals = sum((jnp.sum(exp_value, -1) for exp_value in exp_blocks))[..., None]
    prob_b_blocks = [(exp_value / row_totals).astype(jnp.bfloat16) for exp_value in exp_blocks]

    def attend_block(block):
        return jnp.einsum(
            "hgqk,khd->qhgd",
            prob_b_blocks[block],
            value_block_list[block],
            preferred_element_type=jnp.float32,
        )

    attn_sum = sum((attend_block(block) for block in range(HALO + 1)))
    attn_out = attn_sum.astype(jnp.bfloat16)
    grad_out = output_gradient[0].reshape(output_shape)
    row_delta = jnp.sum(grad_out.astype(jnp.float32) * attn_out.astype(jnp.float32), -1).transpose(
        1, 2, 0
    )

    def backward_block(block):
        prob_grad = jnp.einsum(
            "qhgd,khd->hgqk", grad_out, value_block_list[block], preferred_element_type=jnp.float32
        )
        score_grad = (exp_blocks[block] / row_totals * (prob_grad - row_delta[..., None])).astype(
            jnp.bfloat16
        )
        q_part = jnp.einsum(
            "hgqk,khd->qhgd", score_grad, key_block_list[block], preferred_element_type=jnp.float32
        )
        key_term = (
            jnp.einsum(
                "hgqk,qhgd->khd", score_grad, grouped_queries, preferred_element_type=jnp.float32
            )
            * score_scale
        ).astype(jnp.bfloat16)
        value_term = jnp.einsum(
            "hgqk,qhgd->khd", prob_b_blocks[block], grad_out, preferred_element_type=jnp.float32
        ).astype(jnp.bfloat16)
        return (q_part, key_term, value_term)

    back_blocks = [backward_block(block) for block in range(HALO + 1)]
    q_grad_norm = (sum((item[0] for item in back_blocks)) * score_scale).reshape(
        token_rows, QUERY_HEADS, HEAD_SIZE
    )
    key_acc = back_blocks[HALO][1].astype(jnp.float32)
    value_accumulator = back_blocks[HALO][2].astype(jnp.float32)
    for offset in range(1, HALO + 1):
        block = HALO - offset
        returned = shifted(
            jnp.stack([back_blocks[block][1], back_blocks[block][2]]), "ctx", -offset
        )
        key_acc = key_acc + returned[0].astype(jnp.float32)
        value_accumulator = value_accumulator + returned[1].astype(jnp.float32)
    grad_queries = (
        rms_norm_backward(q_grad_norm, q_normed, q_inv, q_gain)
        .astype(jnp.bfloat16)
        .reshape(1, token_rows, QUERY_HEADS * HEAD_SIZE)
    )
    key_gradient = (
        rms_norm_backward(key_acc, normalized_keys, key_inverse_rms, key_norm_gain)
        .astype(jnp.bfloat16)
        .reshape(1, token_rows, KEY_VALUE_HEADS * HEAD_SIZE)
    )
    value_gradient = value_accumulator.astype(jnp.bfloat16).reshape(
        1, token_rows, KEY_VALUE_HEADS * HEAD_SIZE
    )
    q_sum_part = jnp.sum(q_grad_norm * q_normed, (0, 1))
    k_sum_part = jnp.sum(key_acc * normalized_keys, (0, 1))
    gain_total = butterfly_sum(jnp.concatenate([q_sum_part, k_sum_part]))
    q_total, k_total = gain_total[:HEAD_SIZE], gain_total[HEAD_SIZE:]
    factor = (lax.axis_size("ctx") * lax.axis_size("dp") * token_rows) ** (-0.5)
    return (
        attn_out.reshape(1, token_rows, QUERY_HEADS * HEAD_SIZE),
        grad_queries,
        key_gradient,
        value_gradient,
        q_total * factor,
        k_total * factor,
    )


def solution(mesh):
    placed = (
        P("dp", "ctx", None),
        P("dp", "ctx", None),
        P("dp", "ctx", None),
        P(),
        P(),
        P("dp", "ctx"),
        P("dp", "ctx", None),
    )
    return jax.shard_map(
        body,
        mesh=mesh,
        in_specs=placed,
        out_specs=(
            P("dp", "ctx", None),
            P("dp", "ctx", None),
            P("dp", "ctx", None),
            P("dp", "ctx", None),
            P(),
            P(),
        ),
        check_vma=False,
    )
```

```python
import itertools
import math

import jax
import jax.numpy as jnp
from jax import lax
from jax.sharding import PartitionSpec as P

QUERY_HEADS = 8
KEY_VALUE_HEADS = 4
HEAD_SIZE = 256
WINDOW = 256
HALO = 2


EPS = 1e-06
GAIN_ROUNDS_BEFORE_RETURN = 5


RING_ORDER = {2: (0, 1), 4: (0, 1, 3, 2), 16: (11, 7, 12, 8, 15, 3, 0, 4, 9, 5, 10, 6, 13, 1, 14, 2)}
AXIS_PARTS = {"ctx": (4, 16, 2), "dp": (4, 2)}


def virtual_order(axis, count):
    parts = AXIS_PARTS.get(axis)
    if parts is None or count != math.prod(parts) or any(p not in RING_ORDER for p in parts):
        return list(range(count))
    order = []
    for digits in itertools.product(*[range(p) for p in parts]):
        index = 0
        for digit, size in zip(digits, parts):
            index = index * size + RING_ORDER[size][digit]
        order.append(index)
    return order


def butterfly_rounds():
    rounds = []
    for axis in ("dp", "ctx"):
        count = lax.axis_size(axis)
        if count & (count - 1):
            rounds.append((axis, None))
            continue
        device_of = virtual_order(axis, count)
        virtual_of = {device: virtual for virtual, device in enumerate(device_of)}
        bit = 1
        while bit < count:
            pairs = [(device, device_of[virtual_of[device] ^ bit]) for device in range(count)]
            rounds.append((axis, pairs))
            bit *= 2
    return rounds


def apply_rounds(value, rounds):
    for axis, pairs in rounds:
        if pairs is None:
            value = lax.psum(value, axis)
        else:
            value = value + lax.ppermute(value, axis, pairs)
    return value


def shifted(value, axis, by):
    count = lax.axis_size(axis)
    pairs = [(i, i + by) for i in range(count) if 0 <= i + by < count]
    return lax.ppermute(value, axis, pairs)


def rms_normalize(inputs, heads, gain_vec):
    as_float = inputs.astype(jnp.float32).reshape(inputs.shape[0], heads, HEAD_SIZE)
    inv_rms = lax.rsqrt(jnp.mean(as_float * as_float, -1, keepdims=True) + EPS)
    normed = as_float * inv_rms
    return (normed, inv_rms, (normed * gain_vec).astype(jnp.bfloat16))


def rms_norm_backward(upstream, normed, inv_rms, gain_vec):
    scaled = upstream * gain_vec
    return inv_rms * (scaled - normed * jnp.mean(scaled * normed, -1, keepdims=True))


def body(queries, keys, values, q_gain, key_norm_gain, segment_ids, output_gradient):
    token_rows = queries.shape[1]
    query_group_width = QUERY_HEADS // KEY_VALUE_HEADS
    score_scale = HEAD_SIZE ** (-0.5)
    ctx_index = lax.axis_index("ctx")
    q_normed, q_inv, query_norm_result = rms_normalize(queries[0], QUERY_HEADS, q_gain)
    normalized_keys, key_inverse_rms, key_norm_result = rms_normalize(
        keys[0], KEY_VALUE_HEADS, key_norm_gain
    )
    own_seg = segment_ids[0]
    local_key_value = jnp.stack([keys[0], values[0]])
    received = []
    for offset in range(1, HALO + 1):
        received.append(shifted((local_key_value, own_seg), "ctx", offset))
    blocks = [received[HALO - 1 - block] for block in range(HALO)] + [(local_key_value, own_seg)]
    positions = jnp.arange(token_rows, dtype=jnp.int32)
    q_pos = ctx_index * token_rows + positions
    grouped_queries = query_norm_result.reshape(
        token_rows, KEY_VALUE_HEADS, query_group_width, HEAD_SIZE
    )
    key_block_list, value_block_list, key_masks, live_flags = ([], [], [], [])
    key_hat_list = []
    for block in range(HALO + 1):
        key_value_pair, seg_block = blocks[block]
        if block == HALO:
            block_hat, block_norm = normalized_keys, key_norm_result
        else:
            block_hat, _, block_norm = rms_normalize(
                key_value_pair[0], KEY_VALUE_HEADS, key_norm_gain
            )
        key_hat_list.append(block_hat)
        k_pos = (ctx_index - HALO + block) * token_rows + positions
        distance = q_pos[:, None] - k_pos[None, :]
        key_mask = (
            (distance >= 0)
            & (distance < WINDOW)
            & (k_pos[None, :] >= 0)
            & (own_seg[:, None] == seg_block[None, :])
        )
        key_block_list.append(block_norm)
        value_block_list.append(key_value_pair[1].reshape(token_rows, KEY_VALUE_HEADS, HEAD_SIZE))
        key_masks.append(key_mask)
        live_flags.append(jnp.any(key_mask))
    output_shape = (token_rows, KEY_VALUE_HEADS, query_group_width, HEAD_SIZE)

    def exp_block(block):
        scores = (
            jnp.einsum(
                "qhgd,khd->hgqk",
                grouped_queries,
                key_block_list[block],
                preferred_element_type=jnp.float32,
            )
            * score_scale
        )
        return jnp.where(key_masks[block], jnp.exp(scores), 0.0)

    exp_blocks = [exp_block(block) for block in range(HALO + 1)]
    row_totals = sum((jnp.sum(exp_value, -1) for exp_value in exp_blocks))[..., None]
    prob_b_blocks = [(exp_value / row_totals).astype(jnp.bfloat16) for exp_value in exp_blocks]

    def attend_block(block):
        return jnp.einsum(
            "hgqk,khd->qhgd",
            prob_b_blocks[block],
            value_block_list[block],
            preferred_element_type=jnp.float32,
        )

    attn_sum = sum((attend_block(block) for block in range(HALO + 1)))
    attn_out = attn_sum.astype(jnp.bfloat16)
    grad_out = output_gradient[0].reshape(output_shape)
    row_delta = jnp.sum(grad_out.astype(jnp.float32) * attn_out.astype(jnp.float32), -1).transpose(
        1, 2, 0
    )

    def backward_block(block):
        prob_grad = jnp.einsum(
            "qhgd,khd->hgqk", grad_out, value_block_list[block], preferred_element_type=jnp.float32
        )
        score_grad = (exp_blocks[block] / row_totals * (prob_grad - row_delta[..., None])).astype(
            jnp.bfloat16
        )
        q_part = jnp.einsum(
            "hgqk,khd->qhgd", score_grad, key_block_list[block], preferred_element_type=jnp.float32
        )
        key_term = (
            jnp.einsum(
                "hgqk,qhgd->khd", score_grad, grouped_queries, preferred_element_type=jnp.float32
            )
            * score_scale
        ).astype(jnp.bfloat16)
        value_term = jnp.einsum(
            "hgqk,qhgd->khd", prob_b_blocks[block], grad_out, preferred_element_type=jnp.float32
        ).astype(jnp.bfloat16)
        return (q_part, key_term, value_term)

    back_blocks = [backward_block(block) for block in range(HALO + 1)]
    q_grad_norm = (sum((item[0] for item in back_blocks)) * score_scale).reshape(
        token_rows, QUERY_HEADS, HEAD_SIZE
    )
    q_sum_part = jnp.sum(q_grad_norm * q_normed, (0, 1))
    k_sum_part = sum(
        jnp.sum(back_blocks[block][1].astype(jnp.float32) * key_hat_list[block], (0, 1))
        for block in range(HALO + 1)
    )
    rounds = butterfly_rounds()
    split = min(GAIN_ROUNDS_BEFORE_RETURN, len(rounds))
    gain_partial = apply_rounds(jnp.concatenate([q_sum_part, k_sum_part]), rounds[:split])
    returned_list = [
        shifted(jnp.stack([back_blocks[HALO - offset][1], back_blocks[HALO - offset][2]]), "ctx", -offset)
        for offset in range(1, HALO + 1)
    ]
    returned_list, gain_partial = lax.optimization_barrier((returned_list, gain_partial))
    gain_total = apply_rounds(gain_partial, rounds[split:])
    q_total, k_total = gain_total[:HEAD_SIZE], gain_total[HEAD_SIZE:]
    key_acc = back_blocks[HALO][1].astype(jnp.float32)
    value_accumulator = back_blocks[HALO][2].astype(jnp.float32)
    for returned in returned_list:
        key_acc = key_acc + returned[0].astype(jnp.float32)
        value_accumulator = value_accumulator + returned[1].astype(jnp.float32)
    grad_queries = (
        rms_norm_backward(q_grad_norm, q_normed, q_inv, q_gain)
        .astype(jnp.bfloat16)
        .reshape(1, token_rows, QUERY_HEADS * HEAD_SIZE)
    )
    key_gradient = (
        rms_norm_backward(key_acc, normalized_keys, key_inverse_rms, key_norm_gain)
        .astype(jnp.bfloat16)
        .reshape(1, token_rows, KEY_VALUE_HEADS * HEAD_SIZE)
    )
    value_gradient = value_accumulator.astype(jnp.bfloat16).reshape(
        1, token_rows, KEY_VALUE_HEADS * HEAD_SIZE
    )
    factor = (lax.axis_size("ctx") * lax.axis_size("dp") * token_rows) ** (-0.5)
    return (
        attn_out.reshape(1, token_rows, QUERY_HEADS * HEAD_SIZE),
        grad_queries,
        key_gradient,
        value_gradient,
        q_total * factor,
        k_total * factor,
    )


def solution(mesh):
    placed = (
        P("dp", "ctx", None),
        P("dp", "ctx", None),
        P("dp", "ctx", None),
        P(),
        P(),
        P("dp", "ctx"),
        P("dp", "ctx", None),
    )
    return jax.shard_map(
        body,
        mesh=mesh,
        in_specs=placed,
        out_specs=(
            P("dp", "ctx", None),
            P("dp", "ctx", None),
            P("dp", "ctx", None),
            P("dp", "ctx", None),
            P(),
            P(),
        ),
        check_vma=False,
    )
```

```python
import itertools
import math

import jax
import jax.numpy as jnp
from jax import lax
from jax.sharding import PartitionSpec as P

QUERY_HEADS = 8
KEY_VALUE_HEADS = 4
HEAD_SIZE = 256
WINDOW = 256
HALO = 2


EPS = 1e-06
GAIN_ROUNDS_BEFORE_RETURN = 5


RING_ORDER = {2: (0, 1), 4: (0, 1, 3, 2), 16: (11, 7, 12, 8, 15, 3, 0, 4, 9, 5, 10, 6, 13, 1, 14, 2)}
AXIS_PARTS = {"ctx": (4, 16, 2), "dp": (4, 2)}


def virtual_order(axis, count):
    parts = AXIS_PARTS.get(axis)
    if parts is None or count != math.prod(parts) or any(p not in RING_ORDER for p in parts):
        return list(range(count))
    order = []
    for digits in itertools.product(*[range(p) for p in parts]):
        index = 0
        for digit, size in zip(digits, parts):
            index = index * size + RING_ORDER[size][digit]
        order.append(index)
    return order


def butterfly_rounds():
    rounds = []
    for axis in ("dp", "ctx"):
        count = lax.axis_size(axis)
        if count & (count - 1):
            rounds.append((axis, None))
            continue
        device_of = virtual_order(axis, count)
        virtual_of = {device: virtual for virtual, device in enumerate(device_of)}
        bit = 1
        while bit < count:
            pairs = [(device, device_of[virtual_of[device] ^ bit]) for device in range(count)]
            rounds.append((axis, pairs))
            bit *= 2
    return rounds


def tree_sum(parts):
    while len(parts) > 1:
        paired = [parts[i] + parts[i + 1] for i in range(0, len(parts) - 1, 2)]
        parts = paired + parts[len(parts) - len(parts) % 2 :]
    return parts[0]


def group_sum(value, axis):
    count = lax.axis_size(axis)
    gathered = lax.all_to_all(jnp.broadcast_to(value, (count,) + value.shape), axis, 0, 0)
    return tree_sum([gathered[i] for i in range(count)])


def apply_rounds(value, rounds):
    for axis, pairs in rounds:
        if pairs is None:
            value = lax.psum(value, axis)
        else:
            value = value + lax.ppermute(value, axis, pairs)
    return value


def shifted(value, axis, by):
    count = lax.axis_size(axis)
    pairs = [(i, i + by) for i in range(count) if 0 <= i + by < count]
    return lax.ppermute(value, axis, pairs)


def rms_normalize(inputs, heads, gain_vec):
    as_float = inputs.astype(jnp.float32).reshape(inputs.shape[0], heads, HEAD_SIZE)
    inv_rms = lax.rsqrt(jnp.mean(as_float * as_float, -1, keepdims=True) + EPS)
    normed = as_float * inv_rms
    return (normed, inv_rms, (normed * gain_vec).astype(jnp.bfloat16))


def rms_norm_backward(upstream, normed, inv_rms, gain_vec):
    scaled = upstream * gain_vec
    return inv_rms * (scaled - normed * jnp.mean(scaled * normed, -1, keepdims=True))


def body(queries, keys, values, q_gain, key_norm_gain, segment_ids, output_gradient):
    token_rows = queries.shape[1]
    query_group_width = QUERY_HEADS // KEY_VALUE_HEADS
    score_scale = HEAD_SIZE ** (-0.5)
    ctx_index = lax.axis_index("ctx")
    q_normed, q_inv, query_norm_result = rms_normalize(queries[0], QUERY_HEADS, q_gain)
    normalized_keys, key_inverse_rms, key_norm_result = rms_normalize(
        keys[0], KEY_VALUE_HEADS, key_norm_gain
    )
    own_seg = segment_ids[0]
    local_key_value = jnp.stack([keys[0], values[0]])
    received = []
    for offset in range(1, HALO + 1):
        received.append(shifted((local_key_value, own_seg), "ctx", offset))
    blocks = [received[HALO - 1 - block] for block in range(HALO)] + [(local_key_value, own_seg)]
    positions = jnp.arange(token_rows, dtype=jnp.int32)
    q_pos = ctx_index * token_rows + positions
    grouped_queries = query_norm_result.reshape(
        token_rows, KEY_VALUE_HEADS, query_group_width, HEAD_SIZE
    )
    key_block_list, value_block_list, key_masks, live_flags = ([], [], [], [])
    key_hat_list = []
    for block in range(HALO + 1):
        key_value_pair, seg_block = blocks[block]
        if block == HALO:
            block_hat, block_norm = normalized_keys, key_norm_result
        else:
            block_hat, _, block_norm = rms_normalize(
                key_value_pair[0], KEY_VALUE_HEADS, key_norm_gain
            )
        key_hat_list.append(block_hat)
        k_pos = (ctx_index - HALO + block) * token_rows + positions
        distance = q_pos[:, None] - k_pos[None, :]
        key_mask = (
            (distance >= 0)
            & (distance < WINDOW)
            & (k_pos[None, :] >= 0)
            & (own_seg[:, None] == seg_block[None, :])
        )
        key_block_list.append(block_norm)
        value_block_list.append(key_value_pair[1].reshape(token_rows, KEY_VALUE_HEADS, HEAD_SIZE))
        key_masks.append(key_mask)
        live_flags.append(jnp.any(key_mask))
    output_shape = (token_rows, KEY_VALUE_HEADS, query_group_width, HEAD_SIZE)

    def exp_block(block):
        scores = (
            jnp.einsum(
                "qhgd,khd->hgqk",
                grouped_queries,
                key_block_list[block],
                preferred_element_type=jnp.float32,
            )
            * score_scale
        )
        return jnp.where(key_masks[block], jnp.exp(scores), 0.0)

    exp_blocks = [exp_block(block) for block in range(HALO + 1)]
    row_totals = sum((jnp.sum(exp_value, -1) for exp_value in exp_blocks))[..., None]
    prob_b_blocks = [(exp_value / row_totals).astype(jnp.bfloat16) for exp_value in exp_blocks]

    def attend_block(block):
        return jnp.einsum(
            "hgqk,khd->qhgd",
            prob_b_blocks[block],
            value_block_list[block],
            preferred_element_type=jnp.float32,
        )

    attn_sum = sum((attend_block(block) for block in range(HALO + 1)))
    attn_out = attn_sum.astype(jnp.bfloat16)
    grad_out = output_gradient[0].reshape(output_shape)
    row_delta = jnp.sum(grad_out.astype(jnp.float32) * attn_out.astype(jnp.float32), -1).transpose(
        1, 2, 0
    )

    def backward_block(block):
        prob_grad = jnp.einsum(
            "qhgd,khd->hgqk", grad_out, value_block_list[block], preferred_element_type=jnp.float32
        )
        score_grad = (exp_blocks[block] / row_totals * (prob_grad - row_delta[..., None])).astype(
            jnp.bfloat16
        )
        q_part = jnp.einsum(
            "hgqk,khd->qhgd", score_grad, key_block_list[block], preferred_element_type=jnp.float32
        )
        key_term = (
            jnp.einsum(
                "hgqk,qhgd->khd", score_grad, grouped_queries, preferred_element_type=jnp.float32
            )
            * score_scale
        ).astype(jnp.bfloat16)
        value_term = jnp.einsum(
            "hgqk,qhgd->khd", prob_b_blocks[block], grad_out, preferred_element_type=jnp.float32
        ).astype(jnp.bfloat16)
        return (q_part, key_term, value_term)

    back_blocks = [backward_block(block) for block in range(HALO + 1)]
    q_grad_norm = (sum((item[0] for item in back_blocks)) * score_scale).reshape(
        token_rows, QUERY_HEADS, HEAD_SIZE
    )
    q_sum_part = jnp.sum(q_grad_norm * q_normed, (0, 1))
    k_sum_part = sum(
        jnp.sum(back_blocks[block][1].astype(jnp.float32) * key_hat_list[block], (0, 1))
        for block in range(HALO + 1)
    )
    gain_partial = group_sum(jnp.concatenate([q_sum_part, k_sum_part]), "dp")
    returned_list = [
        shifted(jnp.stack([back_blocks[HALO - offset][1], back_blocks[HALO - offset][2]]), "ctx", -offset)
        for offset in range(1, HALO + 1)
    ]
    returned_list, gain_partial = lax.optimization_barrier((returned_list, gain_partial))
    gain_total = group_sum(gain_partial, "ctx")
    q_total, k_total = gain_total[:HEAD_SIZE], gain_total[HEAD_SIZE:]
    key_acc = back_blocks[HALO][1].astype(jnp.float32)
    value_accumulator = back_blocks[HALO][2].astype(jnp.float32)
    for returned in returned_list:
        key_acc = key_acc + returned[0].astype(jnp.float32)
        value_accumulator = value_accumulator + returned[1].astype(jnp.float32)
    grad_queries = (
        rms_norm_backward(q_grad_norm, q_normed, q_inv, q_gain)
        .astype(jnp.bfloat16)
        .reshape(1, token_rows, QUERY_HEADS * HEAD_SIZE)
    )
    key_gradient = (
        rms_norm_backward(key_acc, normalized_keys, key_inverse_rms, key_norm_gain)
        .astype(jnp.bfloat16)
        .reshape(1, token_rows, KEY_VALUE_HEADS * HEAD_SIZE)
    )
    value_gradient = value_accumulator.astype(jnp.bfloat16).reshape(
        1, token_rows, KEY_VALUE_HEADS * HEAD_SIZE
    )
    factor = (lax.axis_size("ctx") * lax.axis_size("dp") * token_rows) ** (-0.5)
    return (
        attn_out.reshape(1, token_rows, QUERY_HEADS * HEAD_SIZE),
        grad_queries,
        key_gradient,
        value_gradient,
        q_total * factor,
        k_total * factor,
    )


def solution(mesh):
    placed = (
        P("dp", "ctx", None),
        P("dp", "ctx", None),
        P("dp", "ctx", None),
        P(),
        P(),
        P("dp", "ctx"),
        P("dp", "ctx", None),
    )
    return jax.shard_map(
        body,
        mesh=mesh,
        in_specs=placed,
        out_specs=(
            P("dp", "ctx", None),
            P("dp", "ctx", None),
            P("dp", "ctx", None),
            P("dp", "ctx", None),
            P(),
            P(),
        ),
        check_vma=False,
    )
```

```python
import jax
import jax.numpy as jnp
from jax import lax
from jax.sharding import PartitionSpec as P


QUERY_HEADS = 8
KEY_VALUE_HEADS = 4
HEAD_SIZE = 256
WINDOW = 256
HALO = 2


EPS = 1e-06


def tree_sum(parts):
    while len(parts) > 1:
        paired = [parts[i] + parts[i + 1] for i in range(0, len(parts) - 1, 2)]
        parts = paired + parts[len(parts) - len(parts) % 2 :]
    return parts[0]


def group_sum(value, axis):
    count = lax.axis_size(axis)
    gathered = lax.all_to_all(jnp.broadcast_to(value, (count,) + value.shape), axis, 0, 0)
    return tree_sum([gathered[i] for i in range(count)])


def shifted(value, axis, by):
    count = lax.axis_size(axis)
    pairs = [(i, i + by) for i in range(count) if 0 <= i + by < count]
    return lax.ppermute(value, axis, pairs)


def rms_normalize(inputs, heads, gain_vec):
    as_float = inputs.astype(jnp.float32).reshape(inputs.shape[0], heads, HEAD_SIZE)
    inv_rms = lax.rsqrt(jnp.mean(as_float * as_float, -1, keepdims=True) + EPS)
    normed = as_float * inv_rms
    return (normed, inv_rms, (normed * gain_vec).astype(jnp.bfloat16))


def rms_norm_backward(upstream, normed, inv_rms, gain_vec):
    scaled = upstream * gain_vec
    return inv_rms * (scaled - normed * jnp.mean(scaled * normed, -1, keepdims=True))


def body(queries, keys, values, q_gain, key_norm_gain, segment_ids, output_gradient):
    token_rows = queries.shape[1]
    query_group_width = QUERY_HEADS // KEY_VALUE_HEADS
    score_scale = HEAD_SIZE ** (-0.5)
    ctx_index = lax.axis_index("ctx")
    q_normed, q_inv, query_norm_result = rms_normalize(queries[0], QUERY_HEADS, q_gain)
    normalized_keys, key_inverse_rms, key_norm_result = rms_normalize(
        keys[0], KEY_VALUE_HEADS, key_norm_gain
    )
    own_seg = segment_ids[0]
    local_key_value = jnp.stack([keys[0], values[0]])
    received = []
    for offset in range(1, HALO + 1):
        received.append(shifted((local_key_value, own_seg), "ctx", offset))
    blocks = [received[HALO - 1 - block] for block in range(HALO)] + [(local_key_value, own_seg)]
    positions = jnp.arange(token_rows, dtype=jnp.int32)
    q_pos = ctx_index * token_rows + positions
    grouped_queries = query_norm_result.reshape(
        token_rows, KEY_VALUE_HEADS, query_group_width, HEAD_SIZE
    )
    key_block_list, value_block_list, key_masks, live_flags = ([], [], [], [])
    key_hat_list = []
    for block in range(HALO + 1):
        key_value_pair, seg_block = blocks[block]
        if block == HALO:
            block_hat, block_norm = normalized_keys, key_norm_result
        else:
            block_hat, _, block_norm = rms_normalize(
                key_value_pair[0], KEY_VALUE_HEADS, key_norm_gain
            )
        key_hat_list.append(block_hat)
        k_pos = (ctx_index - HALO + block) * token_rows + positions
        distance = q_pos[:, None] - k_pos[None, :]
        key_mask = (
            (distance >= 0)
            & (distance < WINDOW)
            & (k_pos[None, :] >= 0)
            & (own_seg[:, None] == seg_block[None, :])
        )
        key_block_list.append(block_norm)
        value_block_list.append(key_value_pair[1].reshape(token_rows, KEY_VALUE_HEADS, HEAD_SIZE))
        key_masks.append(key_mask)
        live_flags.append(jnp.any(key_mask))
    output_shape = (token_rows, KEY_VALUE_HEADS, query_group_width, HEAD_SIZE)

    def exp_block(block):
        scores = (
            jnp.einsum(
                "qhgd,khd->hgqk",
                grouped_queries,
                key_block_list[block],
                preferred_element_type=jnp.float32,
            )
            * score_scale
        )
        return jnp.where(key_masks[block], jnp.exp(scores), 0.0)

    exp_blocks = [exp_block(block) for block in range(HALO + 1)]
    row_totals = sum((jnp.sum(exp_value, -1) for exp_value in exp_blocks))[..., None]
    prob_b_blocks = [(exp_value / row_totals).astype(jnp.bfloat16) for exp_value in exp_blocks]

    def attend_block(block):
        return jnp.einsum(
            "hgqk,khd->qhgd",
            prob_b_blocks[block],
            value_block_list[block],
            preferred_element_type=jnp.float32,
        )

    attn_sum = sum((attend_block(block) for block in range(HALO + 1)))
    attn_out = attn_sum.astype(jnp.bfloat16)
    grad_out = output_gradient[0].reshape(output_shape)
    row_delta = jnp.sum(grad_out.astype(jnp.float32) * attn_out.astype(jnp.float32), -1).transpose(
        1, 2, 0
    )

    def backward_block(block):
        prob_grad = jnp.einsum("qhgd,khd->hgqk", grad_out, value_block_list[block], preferred_element_type=jnp.float32)
        score_grad = (exp_blocks[block] / row_totals * (prob_grad - row_delta[..., None])).astype(
            jnp.bfloat16
        )
        q_part = jnp.einsum(
            "hgqk,khd->qhgd", score_grad, key_block_list[block], preferred_element_type=jnp.float32
        )
        key_term = (
            jnp.einsum(
                "hgqk,qhgd->khd", score_grad, grouped_queries, preferred_element_type=jnp.float32
            )
            * score_scale
        ).astype(jnp.bfloat16)
        value_term = jnp.einsum(
            "hgqk,qhgd->khd", prob_b_blocks[block], grad_out, preferred_element_type=jnp.float32
        ).astype(jnp.bfloat16)
        return (q_part, key_term, value_term)

    back_blocks = [backward_block(block) for block in range(HALO + 1)]
    value_returns = [
        shifted(back_blocks[HALO - offset][2], "ctx", -offset) for offset in range(1, HALO + 1)
    ]
    q_grad_norm = (sum((item[0] for item in back_blocks)) * score_scale).reshape(
        token_rows, QUERY_HEADS, HEAD_SIZE
    )
    q_sum_part = jnp.sum(q_grad_norm * q_normed, (0, 1))
    k_sum_part = sum(
        jnp.sum(back_blocks[block][1].astype(jnp.float32) * key_hat_list[block], (0, 1))
        for block in range(HALO + 1)
    )
    gain_partial = group_sum(jnp.concatenate([q_sum_part, k_sum_part]), "dp")
    far_key_return = shifted(back_blocks[0][1], "ctx", -HALO)
    returned_list = [
        (
            far_key_return if offset == HALO else shifted(back_blocks[HALO - offset][1], "ctx", -offset),
            value_returns[offset - 1],
        )
        for offset in range(1, HALO + 1)
    ]
    returned_list, gain_partial = lax.optimization_barrier((returned_list, gain_partial))
    gain_total = group_sum(gain_partial, "ctx")
    q_total, k_total = gain_total[:HEAD_SIZE], gain_total[HEAD_SIZE:]
    key_acc = back_blocks[HALO][1].astype(jnp.float32)
    value_accumulator = back_blocks[HALO][2].astype(jnp.float32)
    for returned in returned_list:
        key_acc = key_acc + returned[0].astype(jnp.float32)
        value_accumulator = value_accumulator + returned[1].astype(jnp.float32)
    grad_queries = (
        rms_norm_backward(q_grad_norm, q_normed, q_inv, q_gain)
        .astype(jnp.bfloat16)
        .reshape(1, token_rows, QUERY_HEADS * HEAD_SIZE)
    )
    key_gradient = (
        rms_norm_backward(key_acc, normalized_keys, key_inverse_rms, key_norm_gain)
        .astype(jnp.bfloat16)
        .reshape(1, token_rows, KEY_VALUE_HEADS * HEAD_SIZE)
    )
    value_gradient = value_accumulator.astype(jnp.bfloat16).reshape(
        1, token_rows, KEY_VALUE_HEADS * HEAD_SIZE
    )
    factor = (lax.axis_size("ctx") * lax.axis_size("dp") * token_rows) ** (-0.5)
    return (
        attn_out.reshape(1, token_rows, QUERY_HEADS * HEAD_SIZE),
        grad_queries,
        key_gradient,
        value_gradient,
        q_total * factor,
        k_total * factor,
    )


def solution(mesh):
    placed = (
        P("dp", "ctx", None),
        P("dp", "ctx", None),
        P("dp", "ctx", None),
        P(),
        P(),
        P("dp", "ctx"),
        P("dp", "ctx", None),
    )
    return jax.shard_map(
        body,
        mesh=mesh,
        in_specs=placed,
        out_specs=(
            P("dp", "ctx", None),
            P("dp", "ctx", None),
            P("dp", "ctx", None),
            P("dp", "ctx", None),
            P(),
            P(),
        ),
        check_vma=False,
    )
```
